256 devices in a mesh: row: 8 (over z), col: 32 (over y, x, core).
Axes of the slice: x: 4, y: 4, z: 8, core: 2. Of those that a mesh axis runs over, the one named last changes fastest.
Arguments:
- embeds: bfloat16 [24576, 768], P('col'), may hold values from -6 to 6
- labels: bfloat16 [24576, 1000], P('col'), may hold values from -6 to 6
- sharpness: float32 [24576], P('col'), may hold values from 0.5 to 100
- pattern: int32 [192, 16], P('col'), may hold values from 0 to 191, as said below
- mask_pos: int32 [24576, 50], P('col'), may hold values from 0 to 2047, as said below
Outputs:
- propagated: bfloat16 [24576, 1000], P('col', 'row')
The draws below stay inside these ranges and needn't reach their ends.
Inputs may be any that keep to these rules, and one draw needn't show every extreme that they name: `pattern`: split the row blocks into runs of 6 and the slots into runs of 2; within one run of row blocks and one run of slots, ids that lie in the same run of 6 block ids are equal. `mask_pos`: the 50 positions of a row are distinct; position k * 128 + m names row m of the row block's k-th candidate block.
All inputs are finite; a program needn't handle non-finite values.
Results may differ from the reference program's by a relative error of at most 0.012.
Values may be sent and summed in bfloat16 or wider, within the bound.
No kernel may reach another device: no remote copies, remote signals or barrier semaphores. Data moves between devices by JAX's collectives and lax.ppermute only.
A program may use at most 128 MiB of HBM per device.

```python
import math
import jax
import jax.numpy as jnp
from jax import lax

D = 768
C = 1000
BLOCK = 128
SLOTS = 16
NEIGHBOURS = 50
CANDIDATES = 2048
ROWS = 24576
BLOCKS = 192
BLOCKS_COL = 6
SLOTS_DEV = 2


def draw_sharpness(key, part):
    first_key = jax.random.fold_in(jax.random.fold_in(key, 3), 0)
    base = jnp.exp(jax.random.uniform(first_key, (ROWS,), jnp.float32, math.log(0.5), math.log(4.0)))
    return base.astype(jnp.float32)


def draw_pattern(key, part):
    col_count = BLOCKS // BLOCKS_COL
    row_count = SLOTS // SLOTS_DEV
    keys = jax.random.split(jax.random.fold_in(key, 11), 4)
    chosen = jax.random.randint(keys[0], (col_count, row_count, col_count), 0, BLOCKS_COL)
    first_draw = jax.random.randint(keys[1], (BLOCKS, SLOTS), 0, col_count)
    second_draw = jax.random.randint(keys[2], (BLOCKS, SLOTS), 0, col_count)
    hubs = jax.random.permutation(keys[3], col_count)
    owners = hubs[jnp.minimum(first_draw, second_draw)]
    col_group = (jnp.arange(BLOCKS, dtype=jnp.int32) // BLOCKS_COL)[:, None]
    row_group = (jnp.arange(SLOTS, dtype=jnp.int32) // SLOTS_DEV)[None, :]
    local_ids = chosen[col_group, row_group, owners]
    return (owners * BLOCKS_COL + local_ids).astype(jnp.int32)


def draw_mask_pos(key, part):
    first_key, second_key = jax.random.split(jax.random.fold_in(key, 23), 2)
    stride = CANDIDATES // NEIGHBOURS
    jitter = jax.random.randint(first_key, (ROWS, NEIGHBOURS), 0, stride)
    offset = jax.random.randint(second_key, (ROWS, 1), 0, CANDIDATES)
    steps_base = jnp.arange(NEIGHBOURS, dtype=jnp.int32)[None, :] * stride
    return ((steps_base + jitter + offset) % CANDIDATES).astype(jnp.int32)


def steps_of(key, shape, cuts, least, largest):
    def one(position, shards_of):
        heights = jax.random.uniform(jax.random.fold_in(jax.random.fold_in(key, 6), position), (shards_of,), jnp.float32, least / len(cuts), largest / len(cuts))
        return jnp.repeat(jnp.exp(heights), shape[position] // shards_of).reshape((-1,) + (1,) * (len(shape) - position - 1))

    level = one(*cuts[0])
    for cut in cuts[1:]:
        level = level * one(*cut)
    return level


def scatter_about(key, dims, scale, bound, shards=(), kind=jnp.bfloat16):
    values = jax.random.normal(key, dims, jnp.float32) * scale
    if len(shards) > 0:
        values = steps_of(key, dims, shards, -0.22, 0.18) * values
    return jnp.clip(values, min=-bound, max=bound).astype(kind)


def setup_inputs(seed: int = 0) -> dict:
    arg_keys = jax.random.split(jax.random.key(seed), 6)
    return {
        "embeds": scatter_about(arg_keys[0], (ROWS, D), 1.0, 6.0, ((0, 32),)),
        "labels": scatter_about(arg_keys[1], (ROWS, C), 1.0, 6.0, ((0, 32),)),
        "sharpness": draw_sharpness(jax.random.fold_in(arg_keys[5], 71), 0),
        "pattern": draw_pattern(jax.random.fold_in(arg_keys[5], 71), 0),
        "mask_pos": draw_mask_pos(jax.random.fold_in(arg_keys[5], 71), 0),
    }


mixing = 0.75

def block_weights(query, candidate_ids, sharp, positions):
    scores = jnp.dot(query, candidate_ids.T, preferred_element_type=jnp.float32) / math.sqrt(D)
    logits = scores * sharp[:, None]
    row_ids = jnp.arange(BLOCK, dtype=jnp.int32)[:, None]
    in_mask = jnp.zeros((BLOCK, CANDIDATES), jnp.float32).at[row_ids, positions].set(1.0) > 0.5
    top = lax.optimization_barrier(jnp.max(jnp.where(in_mask, logits, -jnp.inf), axis=1, keepdims=True))
    expo = jnp.where(in_mask, jnp.exp(logits - top), 0.0)
    totals = lax.optimization_barrier(jnp.sum(expo, axis=1, keepdims=True))
    return (expo / totals).astype(jnp.bfloat16)

def blend_label_block(weight_matrix, cand_labels, seed_rows):
    groups = SLOTS // SLOTS_DEV
    wide_w = weight_matrix.astype(jnp.float32).reshape(BLOCK, groups, SLOTS_DEV * BLOCK)
    wide_y = cand_labels.astype(jnp.float32).reshape(groups, SLOTS_DEV * BLOCK, C)
    pieces = jnp.einsum('qgk,gkc->gqc', wide_w, wide_y).astype(jnp.bfloat16)
    pieces = lax.optimization_barrier(pieces)
    summed = lax.optimization_barrier(jnp.sum(pieces.astype(jnp.float32), axis=0))
    return (mixing * summed + (1.0 - mixing) * seed_rows.astype(jnp.float32)).astype(jnp.bfloat16)

def reference(embeds, labels, sharpness, pattern, mask_pos):
    embedding_tiles = embeds.reshape(BLOCKS, BLOCK, D)
    lab_blocks = labels.reshape(BLOCKS, BLOCK, C)
    sharp_blocks = sharpness.reshape(BLOCKS, BLOCK)
    pos_blocks = mask_pos.reshape(BLOCKS, BLOCK, NEIGHBOURS)

    def first_round(index):
        ids = pattern[index]
        candidate_ids = embedding_tiles[ids].reshape(CANDIDATES, D)
        weight_matrix = block_weights(embedding_tiles[index], candidate_ids, sharp_blocks[index], pos_blocks[index])
        spread_rows = blend_label_block(weight_matrix, lab_blocks[ids], lab_blocks[index])
        return (weight_matrix, spread_rows)
    weight_matrix, spread = lax.map(first_round, jnp.arange(BLOCKS, dtype=jnp.int32))

    def second_round(index):
        return blend_label_block(weight_matrix[index], spread[pattern[index]], lab_blocks[index])
    result = lax.map(second_round, jnp.arange(BLOCKS, dtype=jnp.int32))
    return result.reshape(ROWS, C)
```

```python
import math

import jax
import jax.numpy as jnp
from jax import lax
from jax.sharding import PartitionSpec as P

BLOCK = 128
SLOTS = 16


mixing = 0.75
lowest_logit = -1e30


def body(embeds, labels, sharpness, pattern, mask_pos):
    rows_here, width = embeds.shape
    classes = labels.shape[1]
    n_col = lax.axis_size("col")
    n_row = lax.axis_size("row")
    row_pos = lax.axis_index("row")
    blocks_here = rows_here // BLOCK
    slots_here = SLOTS // n_row
    span = slots_here * BLOCK
    my_slots = lax.dynamic_slice_in_dim(pattern, row_pos * slots_here, slots_here, 1)
    owners = my_slots // blocks_here
    local_ids = my_slots % blocks_here
    peers = jnp.arange(n_col, dtype=jnp.int32)
    wanted = jnp.max(jnp.where(owners[..., None] == peers, local_ids[..., None], 0), axis=(0, 1))
    requested = lax.all_to_all(wanted, "col", split_axis=0, concat_axis=0, tiled=True)
    embedding_tiles = embeds.reshape(blocks_here, BLOCK, width)
    lab_blocks = labels.reshape(blocks_here, BLOCK, classes)
    send_emb = embedding_tiles[requested]
    send_lab = lab_blocks[requested]
    shifted = mask_pos - row_pos * span
    shifted = jnp.where((shifted >= 0) & (shifted < span), shifted, span)
    positions = jnp.arange(span, dtype=jnp.int32)
    in_mask = jnp.any(shifted[:, :, None] == positions[None, None, :], axis=1)
    in_mask = in_mask.reshape(blocks_here, BLOCK, span)

    def propagate_using(weight_matrix, fetched_lab):
        candidate_ids = fetched_lab[owners].reshape(blocks_here, span, classes)
        blended_rows = jnp.einsum(
            "tmg,tgh->tmh", weight_matrix, candidate_ids, preferred_element_type=jnp.float32
        )
        return blended_rows.reshape(rows_here, classes)

    fetched_emb, fetched_lab = (
        lax.all_to_all(send_emb, "col", split_axis=0, concat_axis=0, tiled=True),
        lax.all_to_all(send_lab, "col", split_axis=0, concat_axis=0, tiled=True),
    )
    candidate_ids = fetched_emb[owners].reshape(blocks_here, span, width)
    scores = jnp.einsum(
        "evg,erg->evr", embedding_tiles, candidate_ids, preferred_element_type=jnp.float32
    ) / math.sqrt(width)
    logits = scores * sharpness.reshape(blocks_here, BLOCK, 1)
    local_max = jnp.max(jnp.where(in_mask, logits, lowest_logit), axis=2)
    local_sum = jnp.sum(jnp.where(in_mask, jnp.exp(logits - local_max[..., None]), 0.0), axis=2)
    stats = lax.all_gather(jnp.stack([local_max, local_sum]), "row")
    top = jnp.max(stats[:, 0], axis=0)
    totals = jnp.sum(stats[:, 1] * jnp.exp(stats[:, 0] - top), axis=0)
    weight_matrix = jnp.where(
        in_mask, jnp.exp(logits - top[..., None]) / totals[..., None], 0.0
    ).astype(jnp.bfloat16)
    partial_one = propagate_using(weight_matrix, fetched_lab)
    summed = lax.psum(partial_one.astype(jnp.bfloat16), "row").astype(jnp.float32)
    spread = (mixing * summed + (1.0 - mixing) * labels.astype(jnp.float32)).astype(jnp.bfloat16)
    send_spread = spread.reshape(blocks_here, BLOCK, classes)[requested]
    fetched_spread = lax.all_to_all(send_spread, "col", split_axis=0, concat_axis=0, tiled=True)
    partial_two = propagate_using(weight_matrix, fetched_spread)
    share = lax.psum_scatter(
        partial_two.astype(jnp.bfloat16), "row", scatter_dimension=0, tiled=True
    ).astype(jnp.float32)
    rows_dev = rows_here // n_row
    seed_rows = lax.dynamic_slice_in_dim(labels, row_pos * rows_dev, rows_dev, 0)
    mine = (mixing * share + (1.0 - mixing) * seed_rows.astype(jnp.float32)).astype(jnp.bfloat16)
    return lax.all_to_all(mine, "row", split_axis=1, concat_axis=0, tiled=True)


def solution(mesh):
    placed = (P("col", None), P("col", None), P("col"), P("col", None), P("col", None))
    return jax.shard_map(
        body, mesh=mesh, in_specs=placed, out_specs=P("col", "row"), check_vma=False
    )
```

```python
import math

import jax
import jax.numpy as jnp
from jax import lax
from jax.sharding import PartitionSpec as P

BLOCK = 128
SLOTS = 16
CHUNKS = 4


mixing = 0.75
lowest_logit = -1e30


def body(embeds, labels, sharpness, pattern, mask_pos):
    rows_here, width = embeds.shape
    classes = labels.shape[1]
    n_col = lax.axis_size("col")
    n_row = lax.axis_size("row")
    row_pos = lax.axis_index("row")
    blocks_here = rows_here // BLOCK
    slots_here = SLOTS // n_row
    span = slots_here * BLOCK
    my_slots = lax.dynamic_slice_in_dim(pattern, row_pos * slots_here, slots_here, 1)
    owners = my_slots // blocks_here
    local_ids = my_slots % blocks_here
    peers = jnp.arange(n_col, dtype=jnp.int32)
    wanted = jnp.max(jnp.where(owners[..., None] == peers, local_ids[..., None], 0), axis=(0, 1))
    requested = lax.all_to_all(wanted, "col", split_axis=0, concat_axis=0, tiled=True)
    embedding_tiles = embeds.reshape(blocks_here, BLOCK, width)
    send_emb = embedding_tiles[requested]
    shifted = mask_pos - row_pos * span
    shifted = jnp.where((shifted >= 0) & (shifted < span), shifted, span)
    positions = jnp.arange(span, dtype=jnp.int32)
    in_mask = jnp.any(shifted[:, :, None] == positions[None, None, :], axis=1)
    in_mask = in_mask.reshape(blocks_here, BLOCK, span)

    def propagate_using(weight_matrix, fetched_lab):
        width_here = fetched_lab.shape[-1]
        candidate_ids = fetched_lab[owners].reshape(blocks_here, span, width_here)
        blended_rows = jnp.einsum(
            "tmg,tgh->tmh", weight_matrix, candidate_ids, preferred_element_type=jnp.float32
        )
        return blended_rows.reshape(rows_here, width_here)

    fetched_emb = lax.all_to_all(send_emb, "col", split_axis=0, concat_axis=0, tiled=True)
    candidate_ids = fetched_emb[owners].reshape(blocks_here, span, width)
    scores = jnp.einsum(
        "evg,erg->evr", embedding_tiles, candidate_ids, preferred_element_type=jnp.float32
    ) / math.sqrt(width)
    logits = scores * sharpness.reshape(blocks_here, BLOCK, 1)
    local_max = jnp.max(jnp.where(in_mask, logits, lowest_logit), axis=2)
    local_sum = jnp.sum(jnp.where(in_mask, jnp.exp(logits - local_max[..., None]), 0.0), axis=2)
    stats = lax.all_gather(jnp.stack([local_max, local_sum]), "row")
    top = jnp.max(stats[:, 0], axis=0)
    totals = jnp.sum(stats[:, 1] * jnp.exp(stats[:, 0] - top), axis=0)
    weight_matrix = jnp.where(
        in_mask, jnp.exp(logits - top[..., None]) / totals[..., None], 0.0
    ).astype(jnp.bfloat16)
    rows_dev = rows_here // n_row
    piece = classes // CHUNKS
    lab_chunks = labels.reshape(rows_here, CHUNKS, piece).transpose(1, 0, 2)
    fetched = []
    for k in range(CHUNKS):
        send_lab = lab_chunks[k].reshape(blocks_here, BLOCK, piece)[requested]
        fetched.append(lax.all_to_all(send_lab, "col", split_axis=0, concat_axis=0, tiled=True))
    sums = []
    for k in range(CHUNKS):
        partial_one = propagate_using(weight_matrix, fetched[k]).astype(jnp.bfloat16)
        if k > 0:
            partial_one, sums[k - 1] = lax.optimization_barrier((partial_one, sums[k - 1]))
        sums.append(lax.psum(partial_one, "row"))
    spreads = []
    for k in range(CHUNKS):
        summed = sums[k].astype(jnp.float32)
        spread = (mixing * summed + (1.0 - mixing) * lab_chunks[k].astype(jnp.float32)).astype(jnp.bfloat16)
        send_spread = spread.reshape(blocks_here, BLOCK, piece)[requested]
        spreads.append(lax.all_to_all(send_spread, "col", split_axis=0, concat_axis=0, tiled=True))
    shares = []
    for k in range(CHUNKS):
        partial_two = propagate_using(weight_matrix, spreads[k]).astype(jnp.bfloat16)
        if k > 0:
            partial_two, shares[k - 1] = lax.optimization_barrier((partial_two, shares[k - 1]))
        shares.append(lax.psum_scatter(partial_two, "row", scatter_dimension=0, tiled=True))
    outs = []
    for k in range(CHUNKS):
        seed_rows = lax.dynamic_slice_in_dim(lab_chunks[k], row_pos * rows_dev, rows_dev, 0)
        share = shares[k].astype(jnp.float32)
        outs.append((mixing * share + (1.0 - mixing) * seed_rows.astype(jnp.float32)).astype(jnp.bfloat16))
    mine = jnp.concatenate(outs, axis=1)
    return lax.all_to_all(mine, "row", split_axis=1, concat_axis=0, tiled=True)


def solution(mesh):
    placed = (P("col", None), P("col", None), P("col"), P("col", None), P("col", None))
    return jax.shard_map(
        body, mesh=mesh, in_specs=placed, out_specs=P("col", "row"), check_vma=False
    )
```

```python
import math

import jax
import jax.numpy as jnp
from jax import lax
from jax.sharding import PartitionSpec as P

BLOCK = 128
SLOTS = 16


mixing = 0.75
lowest_logit = -1e30


def body(embeds, labels, sharpness, pattern, mask_pos):
    rows_here, width = embeds.shape
    classes = labels.shape[1]
    n_col = lax.axis_size("col")
    n_row = lax.axis_size("row")
    row_pos = lax.axis_index("row")
    blocks_here = rows_here // BLOCK
    slots_here = SLOTS // n_row
    span = slots_here * BLOCK
    per_device = classes // n_row
    owners = pattern // blocks_here
    local_ids = pattern % blocks_here
    peers = jnp.arange(n_col, dtype=jnp.int32)
    grouped_owners = owners.reshape(blocks_here, n_row, slots_here)
    grouped_ids = local_ids.reshape(blocks_here, n_row, slots_here)
    wanted = jnp.max(
        jnp.where(grouped_owners[..., None] == peers, grouped_ids[..., None], 0), axis=(0, 2)
    )
    requested = lax.all_to_all(wanted.T, "col", split_axis=0, concat_axis=0, tiled=True)
    embedding_tiles = embeds.reshape(blocks_here, BLOCK, width)
    send_emb = embedding_tiles[lax.dynamic_index_in_dim(requested, row_pos, 1, keepdims=False)]
    my_labels = lax.dynamic_slice_in_dim(labels, row_pos * per_device, per_device, 1)
    lab_blocks = my_labels.reshape(blocks_here, BLOCK, per_device)
    send_lab = lab_blocks[requested]
    shifted = mask_pos - row_pos * span
    shifted = jnp.where((shifted >= 0) & (shifted < span), shifted, span)
    positions = jnp.arange(span, dtype=jnp.int32)
    in_mask = jnp.any(shifted[:, :, None] == positions[None, None, :], axis=1)
    in_mask = in_mask.reshape(blocks_here, BLOCK, span)

    my_owners = lax.dynamic_slice_in_dim(owners, row_pos * slots_here, slots_here, 1)
    fetched_emb = lax.all_to_all(send_emb, "col", split_axis=0, concat_axis=0, tiled=True)
    fetched_lab = lax.all_to_all(send_lab, "col", split_axis=0, concat_axis=0, tiled=True)
    candidate_ids = fetched_emb[my_owners].reshape(blocks_here, span, width)
    scores = jnp.einsum(
        "evg,erg->evr", embedding_tiles, candidate_ids, preferred_element_type=jnp.float32
    ) / math.sqrt(width)
    logits = scores * sharpness.reshape(blocks_here, BLOCK, 1)
    local_max = jnp.max(jnp.where(in_mask, logits, lowest_logit), axis=2)
    local_sum = jnp.sum(jnp.where(in_mask, jnp.exp(logits - local_max[..., None]), 0.0), axis=2)
    stats = lax.all_gather(jnp.stack([local_max, local_sum]), "row")
    top = jnp.max(stats[:, 0], axis=0)
    totals = jnp.sum(stats[:, 1] * jnp.exp(stats[:, 0] - top), axis=0)
    weight_matrix = jnp.where(
        in_mask, jnp.exp(logits - top[..., None]) / totals[..., None], 0.0
    ).astype(jnp.bfloat16)
    all_weights = lax.all_gather(weight_matrix, "row")
    group_ids = jnp.arange(SLOTS, dtype=jnp.int32) // slots_here

    def propagate_using(fetched, seed):
        candidates = fetched[owners, group_ids[None, :]]
        candidates = candidates.reshape(blocks_here, n_row, span, per_device)
        pieces = jnp.einsum(
            "gtmk,tgkc->gtmc", all_weights, candidates, preferred_element_type=jnp.float32
        ).astype(jnp.bfloat16)
        summed = jnp.sum(pieces.astype(jnp.float32), axis=0).reshape(rows_here, per_device)
        return (mixing * summed + (1.0 - mixing) * seed.astype(jnp.float32)).astype(jnp.bfloat16)

    spread = propagate_using(fetched_lab, my_labels)
    send_spread = spread.reshape(blocks_here, BLOCK, per_device)[requested]
    fetched_spread = lax.all_to_all(send_spread, "col", split_axis=0, concat_axis=0, tiled=True)
    return propagate_using(fetched_spread, my_labels)


def solution(mesh):
    placed = (P("col", None), P("col", None), P("col"), P("col", None), P("col", None))
    return jax.shard_map(
        body, mesh=mesh, in_specs=placed, out_specs=P("col", "row"), check_vma=False
    )
```

```python
import math

import jax
import jax.numpy as jnp
from jax import lax
from jax.sharding import PartitionSpec as P

BLOCK = 128
SLOTS = 16


mixing = 0.75
lowest_logit = -1e30


def body(embeds, labels, sharpness, pattern, mask_pos):
    rows_here, width = embeds.shape
    classes = labels.shape[1]
    n_col = lax.axis_size("col")
    n_row = lax.axis_size("row")
    row_pos = lax.axis_index("row")
    blocks_here = rows_here // BLOCK
    slots_here = SLOTS // n_row
    span = slots_here * BLOCK
    per_device = classes // n_row
    owners = pattern // blocks_here
    local_ids = pattern % blocks_here
    peers = jnp.arange(n_col, dtype=jnp.int32)
    grouped_owners = owners.reshape(blocks_here, n_row, slots_here)
    grouped_ids = local_ids.reshape(blocks_here, n_row, slots_here)
    wanted = jnp.max(
        jnp.where(grouped_owners[..., None] == peers, grouped_ids[..., None], 0), axis=(0, 2)
    )
    requested = lax.all_to_all(wanted.T, "col", split_axis=0, concat_axis=0, tiled=True)
    embedding_tiles = embeds.reshape(blocks_here, BLOCK, width)
    send_emb = embedding_tiles[lax.dynamic_index_in_dim(requested, row_pos, 1, keepdims=False)]
    my_labels = lax.dynamic_slice_in_dim(labels, row_pos * per_device, per_device, 1)
    lanes = -(-per_device // 128) * 128
    padded_labels = jnp.pad(my_labels, ((0, 0), (0, lanes - per_device)))
    lab_blocks = padded_labels.reshape(blocks_here, BLOCK, lanes)
    send_lab = lab_blocks[requested]
    shifted = mask_pos - row_pos * span
    shifted = jnp.where((shifted >= 0) & (shifted < span), shifted, span)
    positions = jnp.arange(span, dtype=jnp.int32)
    in_mask = jnp.any(shifted[:, :, None] == positions[None, None, :], axis=1)
    in_mask = in_mask.reshape(blocks_here, BLOCK, span)

    my_owners = lax.dynamic_slice_in_dim(owners, row_pos * slots_here, slots_here, 1)
    fetched_emb = lax.all_to_all(send_emb, "col", split_axis=0, concat_axis=0, tiled=True)
    fetched_lab = lax.all_to_all(send_lab, "col", split_axis=0, concat_axis=0, tiled=True)
    candidate_ids = fetched_emb[my_owners].reshape(blocks_here, span, width)
    scores = jnp.einsum(
        "evg,erg->evr", embedding_tiles, candidate_ids, preferred_element_type=jnp.float32
    ) / math.sqrt(width)
    logits = scores * sharpness.reshape(blocks_here, BLOCK, 1)
    local_max = jnp.max(jnp.where(in_mask, logits, lowest_logit), axis=2)
    local_sum = jnp.sum(jnp.where(in_mask, jnp.exp(logits - local_max[..., None]), 0.0), axis=2)
    stats = lax.all_gather(jnp.stack([local_max, local_sum]), "row")
    top = jnp.max(stats[:, 0], axis=0)
    totals = jnp.sum(stats[:, 1] * jnp.exp(stats[:, 0] - top), axis=0)
    weight_matrix = jnp.where(
        in_mask, jnp.exp(logits - top[..., None]) / totals[..., None], 0.0
    ).astype(jnp.bfloat16)
    all_weights = lax.all_gather(weight_matrix, "row")
    group_ids = jnp.arange(SLOTS, dtype=jnp.int32) // slots_here

    def propagate_using(fetched, seed):
        candidates = fetched[owners, group_ids[None, :]]
        candidates = candidates.reshape(blocks_here, n_row, span, lanes)
        pieces = jnp.einsum(
            "gtmk,tgkc->gtmc", all_weights, candidates, preferred_element_type=jnp.float32
        ).astype(jnp.bfloat16)
        summed = jnp.sum(pieces.astype(jnp.float32), axis=0).reshape(rows_here, lanes)
        return (mixing * summed + (1.0 - mixing) * seed.astype(jnp.float32)).astype(jnp.bfloat16)

    spread = propagate_using(fetched_lab, padded_labels)
    send_spread = spread.reshape(blocks_here, BLOCK, lanes)[requested]
    fetched_spread = lax.all_to_all(send_spread, "col", split_axis=0, concat_axis=0, tiled=True)
    return propagate_using(fetched_spread, padded_labels)[:, :per_device]


def solution(mesh):
    placed = (P("col", None), P("col", None), P("col"), P("col", None), P("col", None))
    return jax.shard_map(
        body, mesh=mesh, in_specs=placed, out_specs=P("col", "row"), check_vma=False
    )
```

```python
import math

import jax
import jax.numpy as jnp
from jax import lax
from jax.sharding import PartitionSpec as P

BLOCK = 128
SLOTS = 16


mixing = 0.75
lowest_logit = -1e30


def body(embeds, labels, sharpness, pattern, mask_pos):
    rows_here, width = embeds.shape
    classes = labels.shape[1]
    n_col = lax.axis_size("col")
    n_row = lax.axis_size("row")
    row_pos = lax.axis_index("row")
    blocks_here = rows_here // BLOCK
    slots_here = SLOTS // n_row
    span = slots_here * BLOCK
    per_device = classes // n_row
    owners = pattern // blocks_here
    local_ids = pattern % blocks_here
    my_owners = lax.dynamic_slice_in_dim(owners, row_pos * slots_here, slots_here, 1)
    my_ids = lax.dynamic_slice_in_dim(local_ids, row_pos * slots_here, slots_here, 1)
    peers = jnp.arange(n_col, dtype=jnp.int32)
    wanted = jnp.max(jnp.where(my_owners[..., None] == peers, my_ids[..., None], 0), axis=(0, 1))
    requested = lax.all_to_all(wanted, "col", split_axis=0, concat_axis=0, tiled=True)
    embedding_tiles = embeds.reshape(blocks_here, BLOCK, width)
    send_emb = embedding_tiles[requested]
    my_labels = lax.dynamic_slice_in_dim(labels, row_pos * per_device, per_device, 1)
    all_labels = lax.all_gather(my_labels, "col", tiled=True)
    shifted = mask_pos - row_pos * span
    shifted = jnp.where((shifted >= 0) & (shifted < span), shifted, span)
    positions = jnp.arange(span, dtype=jnp.int32)
    in_mask = jnp.any(shifted[:, :, None] == positions[None, None, :], axis=1)
    in_mask = in_mask.reshape(blocks_here, BLOCK, span)

    fetched_emb = lax.all_to_all(send_emb, "col", split_axis=0, concat_axis=0, tiled=True)
    candidate_ids = fetched_emb[my_owners].reshape(blocks_here, span, width)
    scores = jnp.einsum(
        "evg,erg->evr", embedding_tiles, candidate_ids, preferred_element_type=jnp.float32
    ) / math.sqrt(width)
    logits = scores * sharpness.reshape(blocks_here, BLOCK, 1)
    local_max = jnp.max(jnp.where(in_mask, logits, lowest_logit), axis=2)
    local_sum = jnp.sum(jnp.where(in_mask, jnp.exp(logits - local_max[..., None]), 0.0), axis=2)
    stats = lax.all_gather(jnp.stack([local_max, local_sum]), "row")
    top = jnp.max(stats[:, 0], axis=0)
    totals = jnp.sum(stats[:, 1] * jnp.exp(stats[:, 0] - top), axis=0)
    weight_matrix = jnp.where(
        in_mask, jnp.exp(logits - top[..., None]) / totals[..., None], 0.0
    ).astype(jnp.bfloat16)
    all_weights = lax.all_gather(weight_matrix, "row")

    def propagate_using(gathered, seed):
        candidates = gathered.reshape(-1, BLOCK, per_device)[pattern]
        candidates = candidates.reshape(blocks_here, n_row, span, per_device)
        pieces = jnp.einsum(
            "gtmk,tgkc->gtmc", all_weights, candidates, preferred_element_type=jnp.float32
        ).astype(jnp.bfloat16)
        summed = jnp.sum(pieces.astype(jnp.float32), axis=0).reshape(rows_here, per_device)
        return (mixing * summed + (1.0 - mixing) * seed.astype(jnp.float32)).astype(jnp.bfloat16)

    spread = propagate_using(all_labels, my_labels)
    all_spread = lax.all_gather(spread, "col", tiled=True)
    return propagate_using(all_spread, my_labels)


def solution(mesh):
    placed = (P("col", None), P("col", None), P("col"), P("col", None), P("col", None))
    return jax.shard_map(
        body, mesh=mesh, in_specs=placed, out_specs=P("col", "row"), check_vma=False
    )
```

```python
import math

import jax
import jax.numpy as jnp
from jax import lax
from jax.sharding import PartitionSpec as P

BLOCK = 128
SLOTS = 16


mixing = 0.75
lowest_logit = -1e30


COL = ("chip", "core")


def gather_columns(x):
    rows_here, width = x.shape
    same_core = lax.all_gather(x, "chip", tiled=True).reshape(-1, BLOCK, width)
    other_core = lax.ppermute(same_core, "core", [(0, 1), (1, 0)])
    return same_core, other_core


def body(embeds, labels, sharpness, pattern, mask_pos):
    rows_here, width = embeds.shape
    classes = labels.shape[1]
    n_col = lax.axis_size(COL)
    n_row = lax.axis_size("row")
    row_pos = lax.axis_index("row")
    blocks_here = rows_here // BLOCK
    slots_here = SLOTS // n_row
    span = slots_here * BLOCK
    per_device = classes // n_row
    owners = pattern // blocks_here
    local_ids = pattern % blocks_here
    my_owners = lax.dynamic_slice_in_dim(owners, row_pos * slots_here, slots_here, 1)
    my_ids = lax.dynamic_slice_in_dim(local_ids, row_pos * slots_here, slots_here, 1)
    peers = jnp.arange(n_col, dtype=jnp.int32)
    wanted = jnp.max(jnp.where(my_owners[..., None] == peers, my_ids[..., None], 0), axis=(0, 1))
    requested = lax.all_to_all(wanted, COL, split_axis=0, concat_axis=0, tiled=True)
    embedding_tiles = embeds.reshape(blocks_here, BLOCK, width)
    send_emb = embedding_tiles[requested]
    my_labels = lax.dynamic_slice_in_dim(labels, row_pos * per_device, per_device, 1)
    lanes = -(-per_device // 128) * 128
    my_labels = jnp.pad(my_labels, ((0, 0), (0, lanes - per_device)))
    all_labels = gather_columns(my_labels)
    shifted = mask_pos - row_pos * span
    shifted = jnp.where((shifted >= 0) & (shifted < span), shifted, span)
    positions = jnp.arange(span, dtype=jnp.int32)
    in_mask = jnp.any(shifted[:, :, None] == positions[None, None, :], axis=1)
    in_mask = in_mask.reshape(blocks_here, BLOCK, span)

    fetched_emb = lax.all_to_all(send_emb, COL, split_axis=0, concat_axis=0, tiled=True)
    candidate_ids = fetched_emb[my_owners].reshape(blocks_here, span, width)
    scores = jnp.einsum(
        "evg,erg->evr", embedding_tiles, candidate_ids, preferred_element_type=jnp.float32
    ) / math.sqrt(width)
    logits = scores * sharpness.reshape(blocks_here, BLOCK, 1)
    local_max = jnp.max(jnp.where(in_mask, logits, lowest_logit), axis=2)
    local_sum = jnp.sum(jnp.where(in_mask, jnp.exp(logits - local_max[..., None]), 0.0), axis=2)
    stats = lax.all_gather(jnp.stack([local_max, local_sum]), "row")
    top = jnp.max(stats[:, 0], axis=0)
    totals = jnp.sum(stats[:, 1] * jnp.exp(stats[:, 0] - top), axis=0)
    weight_matrix = jnp.where(
        in_mask, jnp.exp(logits - top[..., None]) / totals[..., None], 0.0
    ).astype(jnp.bfloat16)
    all_weights = lax.all_gather(weight_matrix, "row")

    shard_of = pattern // blocks_here
    on_this_core = (shard_of % 2 == lax.axis_index("core"))[..., None, None]
    pair_ids = (shard_of // 2) * blocks_here + pattern % blocks_here

    def propagate_using(gathered, seed):
        same_core, other_core = gathered
        candidates = jnp.where(on_this_core, same_core[pair_ids], other_core[pair_ids])
        candidates = candidates.reshape(blocks_here, n_row, span, lanes)
        pieces = jnp.einsum(
            "gtmk,tgkc->gtmc", all_weights, candidates, preferred_element_type=jnp.float32
        ).astype(jnp.bfloat16)
        summed = jnp.sum(pieces.astype(jnp.float32), axis=0).reshape(rows_here, lanes)
        return (mixing * summed + (1.0 - mixing) * seed.astype(jnp.float32)).astype(jnp.bfloat16)

    spread = propagate_using(all_labels, my_labels)
    all_spread = gather_columns(spread)
    return propagate_using(all_spread, my_labels)[:, :per_device]


def solution(mesh):
    devices = mesh.devices
    fine = jax.sharding.Mesh(
        devices.reshape(devices.shape[0], devices.shape[1] // 2, 2), ("row", "chip", "core")
    )
    placed = (P(COL, None), P(COL, None), P(COL), P(COL, None), P(COL, None))
    return jax.shard_map(
        body, mesh=fine, in_specs=placed, out_specs=P(COL, "row"), check_vma=False
    )
```

```python
import math

import jax
import jax.numpy as jnp
from jax import lax
from jax.sharding import PartitionSpec as P

BLOCK = 128
SLOTS = 16


mixing = 0.75
lowest_logit = -1e30


COL = ("chip", "core")


def gather_columns(x):
    rows_here, width = x.shape
    same_core = lax.all_gather(x, "chip", tiled=True).reshape(-1, BLOCK, width)
    other_core = lax.ppermute(same_core, "core", [(0, 1), (1, 0)])
    return same_core, other_core


def body(embeds, labels, sharpness, pattern, mask_pos):
    rows_here, width = embeds.shape
    classes = labels.shape[1]
    n_col = lax.axis_size(COL)
    n_row = lax.axis_size("row")
    row_pos = lax.axis_index("row")
    blocks_here = rows_here // BLOCK
    slots_here = SLOTS // n_row
    span = slots_here * BLOCK
    per_device = classes // n_row
    owners = pattern // blocks_here
    local_ids = pattern % blocks_here
    my_owners = lax.dynamic_slice_in_dim(owners, row_pos * slots_here, slots_here, 1)
    my_ids = lax.dynamic_slice_in_dim(local_ids, row_pos * slots_here, slots_here, 1)
    peers = jnp.arange(n_col, dtype=jnp.int32)
    wanted = jnp.max(jnp.where(my_owners[..., None] == peers, my_ids[..., None], 0), axis=(0, 1))
    requested = lax.all_to_all(wanted, COL, split_axis=0, concat_axis=0, tiled=True)
    embedding_tiles = embeds.reshape(blocks_here, BLOCK, width)
    send_emb = embedding_tiles[requested]
    my_labels = lax.dynamic_slice_in_dim(labels, row_pos * per_device, per_device, 1)
    lanes = -(-per_device // 128) * 128
    my_labels = jnp.pad(my_labels, ((0, 0), (0, lanes - per_device)))
    all_labels = gather_columns(my_labels)
    shifted = mask_pos - row_pos * span
    shifted = jnp.where((shifted >= 0) & (shifted < span), shifted, span)
    positions = jnp.arange(span, dtype=jnp.int32)
    in_mask = jnp.any(shifted[:, :, None] == positions[None, None, :], axis=1)
    in_mask = in_mask.reshape(blocks_here, BLOCK, span)

    fetched_emb = lax.all_to_all(send_emb, COL, split_axis=0, concat_axis=0, tiled=True)
    candidate_ids = fetched_emb[my_owners].reshape(blocks_here, span, width)
    scores = jnp.einsum(
        "evg,erg->evr", embedding_tiles, candidate_ids, preferred_element_type=jnp.float32
    ) / math.sqrt(width)
    logits = scores * sharpness.reshape(blocks_here, BLOCK, 1)
    local_max = jnp.max(jnp.where(in_mask, logits, lowest_logit), axis=2)
    local_sum = jnp.sum(jnp.where(in_mask, jnp.exp(logits - local_max[..., None]), 0.0), axis=2)
    local_weights = jnp.where(
        in_mask, jnp.exp(logits - local_max[..., None]), 0.0
    ).astype(jnp.bfloat16)
    stats = lax.all_gather(jnp.stack([local_max, local_sum]), "row")
    all_weights = lax.all_gather(local_weights, "row")
    top = jnp.max(stats[:, 0], axis=0)
    totals = jnp.sum(stats[:, 1] * jnp.exp(stats[:, 0] - top), axis=0)
    factors = jnp.exp(stats[:, 0] - top) / totals

    shard_of = pattern // blocks_here
    on_this_core = (shard_of % 2 == lax.axis_index("core"))[..., None, None]
    pair_ids = (shard_of // 2) * blocks_here + pattern % blocks_here

    def propagate_using(gathered, seed):
        same_core, other_core = gathered
        candidates = jnp.where(on_this_core, same_core[pair_ids], other_core[pair_ids])
        candidates = candidates.reshape(blocks_here, n_row, span, lanes)
        pieces = jnp.einsum(
            "gtmk,tgkc->gtmc", all_weights, candidates, preferred_element_type=jnp.float32
        )
        pieces = (pieces * factors[..., None]).astype(jnp.bfloat16)
        summed = jnp.sum(pieces.astype(jnp.float32), axis=0).reshape(rows_here, lanes)
        return (mixing * summed + (1.0 - mixing) * seed.astype(jnp.float32)).astype(jnp.bfloat16)

    spread = propagate_using(all_labels, my_labels)
    all_spread = gather_columns(spread)
    return propagate_using(all_spread, my_labels)[:, :per_device]


def solution(mesh):
    devices = mesh.devices
    fine = jax.sharding.Mesh(
        devices.reshape(devices.shape[0], devices.shape[1] // 2, 2), ("row", "chip", "core")
    )
    placed = (P(COL, None), P(COL, None), P(COL), P(COL, None), P(COL, None))
    return jax.shard_map(
        body, mesh=fine, in_specs=placed, out_specs=P(COL, "row"), check_vma=False
    )
```

```python
import math

import jax
import jax.numpy as jnp
from jax import lax
from jax.sharding import PartitionSpec as P

BLOCK = 128
SLOTS = 16


mixing = 0.75
lowest_logit = -1e30


COL = ("y", "x", "core")


def ring_gather(x, axis):
    n = lax.axis_size(axis)
    ahead, behind = [], []
    cur_f, cur_b = x, x
    for step in range(1, n // 2 + 1):
        cur_f = lax.ppermute(cur_f, axis, [(i, (i + 1) % n) for i in range(n)])
        behind.append(cur_f)
    for step in range(1, (n - 1) // 2 + 1):
        cur_b = lax.ppermute(cur_b, axis, [(i, (i - 1) % n) for i in range(n)])
        ahead.append(cur_b)
    return jnp.stack([x] + ahead + behind[::-1])


def gather_columns(x):
    rows_here, width = x.shape
    along_x = ring_gather(x.reshape(rows_here // BLOCK, BLOCK, width), "x")
    same_core = ring_gather(along_x, "y")
    other_core = lax.ppermute(same_core, "core", [(0, 1), (1, 0)])
    return same_core, other_core


def body(embeds, labels, sharpness, pattern, mask_pos):
    rows_here, width = embeds.shape
    classes = labels.shape[1]
    n_col = lax.axis_size(COL)
    n_row = lax.axis_size("row")
    row_pos = lax.axis_index("row")
    blocks_here = rows_here // BLOCK
    slots_here = SLOTS // n_row
    span = slots_here * BLOCK
    per_device = classes // n_row
    owners = pattern // blocks_here
    local_ids = pattern % blocks_here
    my_owners = lax.dynamic_slice_in_dim(owners, row_pos * slots_here, slots_here, 1)
    my_ids = lax.dynamic_slice_in_dim(local_ids, row_pos * slots_here, slots_here, 1)
    peers = jnp.arange(n_col, dtype=jnp.int32)
    wanted = jnp.max(jnp.where(my_owners[..., None] == peers, my_ids[..., None], 0), axis=(0, 1))
    requested = lax.all_to_all(wanted, COL, split_axis=0, concat_axis=0, tiled=True)
    embedding_tiles = embeds.reshape(blocks_here, BLOCK, width)
    send_emb = embedding_tiles[requested]
    my_labels = lax.dynamic_slice_in_dim(labels, row_pos * per_device, per_device, 1)
    lanes = -(-per_device // 128) * 128
    my_labels = jnp.pad(my_labels, ((0, 0), (0, lanes - per_device)))
    all_labels = gather_columns(my_labels)
    shifted = mask_pos - row_pos * span
    shifted = jnp.where((shifted >= 0) & (shifted < span), shifted, span)
    positions = jnp.arange(span, dtype=jnp.int32)
    in_mask = jnp.any(shifted[:, :, None] == positions[None, None, :], axis=1)
    in_mask = in_mask.reshape(blocks_here, BLOCK, span)

    fetched_emb = lax.all_to_all(send_emb, COL, split_axis=0, concat_axis=0, tiled=True)
    candidate_ids = fetched_emb[my_owners].reshape(blocks_here, span, width)
    scores = jnp.einsum(
        "evg,erg->evr", embedding_tiles, candidate_ids, preferred_element_type=jnp.float32
    ) / math.sqrt(width)
    logits = scores * sharpness.reshape(blocks_here, BLOCK, 1)
    local_max = jnp.max(jnp.where(in_mask, logits, lowest_logit), axis=2)
    local_sum = jnp.sum(jnp.where(in_mask, jnp.exp(logits - local_max[..., None]), 0.0), axis=2)
    local_weights = jnp.where(
        in_mask, jnp.exp(logits - local_max[..., None]), 0.0
    ).astype(jnp.bfloat16)
    stats = ring_gather(jnp.stack([local_max, local_sum]), "row")
    all_weights = ring_gather(local_weights, "row")
    top = jnp.max(stats[:, 0], axis=0)
    totals = jnp.sum(stats[:, 1] * jnp.exp(stats[:, 0] - top), axis=0)
    factors = jnp.exp(stats[:, 0] - top) / totals

    ring_groups = (row_pos + jnp.arange(n_row, dtype=jnp.int32)) % n_row
    slot_order = (ring_groups[:, None] * slots_here + jnp.arange(slots_here, dtype=jnp.int32)).reshape(-1)
    pattern = pattern[:, slot_order]
    n_core = lax.axis_size("core")
    n_x = lax.axis_size("x")
    n_y = lax.axis_size("y")
    shard_of = pattern // blocks_here
    on_this_core = (shard_of % n_core == lax.axis_index("core"))[..., None, None]
    pair_ids = (
        (shard_of // (n_core * n_x) - lax.axis_index("y")) % n_y,
        (shard_of // n_core % n_x - lax.axis_index("x")) % n_x,
        pattern % blocks_here,
    )

    def propagate_using(gathered, seed):
        same_core, other_core = gathered
        candidates = jnp.where(on_this_core, same_core[pair_ids], other_core[pair_ids])
        candidates = candidates.reshape(blocks_here, n_row, span, lanes)
        pieces = jnp.einsum(
            "gtmk,tgkc->gtmc", all_weights, candidates, preferred_element_type=jnp.float32
        )
        pieces = (pieces * factors[..., None]).astype(jnp.bfloat16)
        summed = jnp.sum(pieces.astype(jnp.float32), axis=0).reshape(rows_here, lanes)
        return (mixing * summed + (1.0 - mixing) * seed.astype(jnp.float32)).astype(jnp.bfloat16)

    spread = propagate_using(all_labels, my_labels)
    all_spread = gather_columns(spread)
    return propagate_using(all_spread, my_labels)[:, :per_device]


def solution(mesh):
    devices = mesh.devices
    n_x = len({d.coords[0] for d in devices.reshape(-1)})
    fine = jax.sharding.Mesh(
        devices.reshape(devices.shape[0], devices.shape[1] // (2 * n_x), n_x, 2),
        ("row", "y", "x", "core"),
    )
    placed = (P(COL, None), P(COL, None), P(COL), P(COL, None), P(COL, None))
    return jax.shard_map(
        body, mesh=fine, in_specs=placed, out_specs=P(COL, "row"), check_vma=False
    )
```

```python
import math

import jax
import jax.numpy as jnp
from jax import lax
from jax.sharding import PartitionSpec as P

BLOCK = 128
SLOTS = 16


mixing = 0.75
lowest_logit = -1e30


COL = ("chip", "core")


def gather_columns(x):
    rows_here, width = x.shape
    same_core = lax.all_gather(x, "chip", tiled=True).reshape(-1, BLOCK, width)
    other_core = lax.ppermute(same_core, "core", [(0, 1), (1, 0)])
    return same_core, other_core


def body(embeds, labels, sharpness, pattern, mask_pos):
    rows_here, width = embeds.shape
    classes = labels.shape[1]
    n_col = lax.axis_size(COL)
    n_row = lax.axis_size("row")
    row_pos = lax.axis_index("row")
    blocks_here = rows_here // BLOCK
    slots_here = SLOTS // n_row
    span = slots_here * BLOCK
    per_device = classes // n_row
    owners = pattern // blocks_here
    local_ids = pattern % blocks_here
    my_owners = lax.dynamic_slice_in_dim(owners, row_pos * slots_here, slots_here, 1)
    my_ids = lax.dynamic_slice_in_dim(local_ids, row_pos * slots_here, slots_here, 1)
    peers = jnp.arange(n_col, dtype=jnp.int32)
    wanted = jnp.max(jnp.where(my_owners[..., None] == peers, my_ids[..., None], 0), axis=(0, 1))
    requested = lax.all_to_all(wanted, COL, split_axis=0, concat_axis=0, tiled=True)
    embedding_tiles = embeds.reshape(blocks_here, BLOCK, width)
    send_emb = embedding_tiles[requested]
    my_labels = lax.dynamic_slice_in_dim(labels, row_pos * per_device, per_device, 1)
    lanes = -(-per_device // 128) * 128
    my_labels = jnp.pad(my_labels, ((0, 0), (0, lanes - per_device)))
    all_labels = gather_columns(my_labels)
    shifted = mask_pos - row_pos * span
    shifted = jnp.where((shifted >= 0) & (shifted < span), shifted, span)
    positions = jnp.arange(span, dtype=jnp.int32)
    in_mask = jnp.any(shifted[:, :, None] == positions[None, None, :], axis=1)
    in_mask = in_mask.reshape(blocks_here, BLOCK, span)

    fetched_emb = lax.all_to_all(send_emb, COL, split_axis=0, concat_axis=0, tiled=True)
    candidate_ids = fetched_emb[my_owners].reshape(blocks_here, span, width)
    scores = jnp.einsum(
        "evg,erg->evr", embedding_tiles, candidate_ids, preferred_element_type=jnp.float32
    ) / math.sqrt(width)
    logits = scores * sharpness.reshape(blocks_here, BLOCK, 1)
    local_max = jnp.max(jnp.where(in_mask, logits, lowest_logit), axis=2)
    local_sum = jnp.sum(jnp.where(in_mask, jnp.exp(logits - local_max[..., None]), 0.0), axis=2)
    local_weights = jnp.where(
        in_mask, jnp.exp(logits - local_max[..., None]), 0.0
    ).astype(jnp.bfloat16)
    stats = lax.all_gather(jnp.stack([local_max, local_sum]), "row")
    all_weights = lax.all_gather(local_weights, "row")
    top = jnp.max(stats[:, 0], axis=0)
    totals = jnp.sum(stats[:, 1] * jnp.exp(stats[:, 0] - top), axis=0)
    factors = jnp.exp(stats[:, 0] - top) / totals

    shard_of = pattern // blocks_here
    on_this_core = (shard_of % 2 == lax.axis_index("core"))[..., None, None]
    pair_ids = (shard_of // 2) * blocks_here + pattern % blocks_here

    def propagate_using(gathered, seed, whole=False):
        if whole:
            candidates = gathered[pattern]
        else:
            same_core, other_core = gathered
            candidates = jnp.where(on_this_core, same_core[pair_ids], other_core[pair_ids])
        candidates = candidates.reshape(blocks_here, n_row, span, lanes)
        pieces = jnp.einsum(
            "gtmk,tgkc->gtmc", all_weights, candidates, preferred_element_type=jnp.float32
        )
        pieces = (pieces * factors[..., None]).astype(jnp.bfloat16)
        summed = jnp.sum(pieces.astype(jnp.float32), axis=0).reshape(rows_here, lanes)
        return (mixing * summed + (1.0 - mixing) * seed.astype(jnp.float32)).astype(jnp.bfloat16)

    spread = propagate_using(all_labels, my_labels)
    whole_spread = lax.all_gather(spread, COL, tiled=True).reshape(-1, BLOCK, lanes)
    return propagate_using(whole_spread, my_labels, whole=True)[:, :per_device]


def solution(mesh):
    devices = mesh.devices
    fine = jax.sharding.Mesh(
        devices.reshape(devices.shape[0], devices.shape[1] // 2, 2), ("row", "chip", "core")
    )
    placed = (P(COL, None), P(COL, None), P(COL), P(COL, None), P(COL, None))
    return jax.shard_map(
        body, mesh=fine, in_specs=placed, out_specs=P(COL, "row"), check_vma=False
    )
```

```python
import functools
import math

import jax
import jax.numpy as jnp
from jax import lax
from jax.experimental import pallas as pl
from jax.experimental.pallas import tpu as pltpu
from jax.sharding import PartitionSpec as P

BLOCK = 128
SLOTS = 16


mixing = 0.75
lowest_logit = -1e30


COL = ("chip", "core")


def round_kernel(pat_ref, w_ref, f_ref, seed_ref, table_hbm, out_ref, buf, sems, *, n_blocks, n_groups, per_group, mixing):
    n_slots = n_groups * per_group
    copies = []
    for t in range(n_blocks):
        for slot in range(n_slots):
            idx = t * n_slots + slot
            c = pltpu.make_async_copy(table_hbm.at[pat_ref[t, slot]], buf.at[idx], sems.at[idx])
            c.start()
            copies.append(c)
    bl = buf.shape[1]
    for t in range(n_blocks):
        total = jnp.zeros(out_ref.shape[1:], jnp.float32)
        for g in range(n_groups):
            acc = jnp.zeros(out_ref.shape[1:], jnp.float32)
            for s in range(per_group):
                idx = t * n_slots + g * per_group + s
                copies[idx].wait()
                acc = acc + jnp.dot(w_ref[g, t, :, s * bl:(s + 1) * bl], buf[idx], preferred_element_type=jnp.float32)
            total = total + (acc * f_ref[g, t]).astype(jnp.bfloat16).astype(jnp.float32)
        out_ref[t] = (mixing * total + (1.0 - mixing) * seed_ref[t].astype(jnp.float32)).astype(out_ref.dtype)

def fused_round(pattern, weights, factors, seed, table, mixing=0.75, interpret=False):
    n_groups, n_blocks, bl, span = weights.shape
    per_group = span // bl
    lanes = table.shape[-1]
    n_slots = n_groups * per_group
    kern = functools.partial(round_kernel, n_blocks=n_blocks, n_groups=n_groups, per_group=per_group, mixing=mixing)
    return pl.pallas_call(
        kern,
        out_shape=jax.ShapeDtypeStruct((n_blocks, bl, lanes), seed.dtype),
        grid_spec=pltpu.PrefetchScalarGridSpec(
            num_scalar_prefetch=1,
            grid=(1,),
            in_specs=[
                pl.BlockSpec(weights.shape, lambda i, p: (0, 0, 0, 0)),
                pl.BlockSpec(factors.shape, lambda i, p: (0, 0, 0, 0)),
                pl.BlockSpec(seed.shape, lambda i, p: (0, 0, 0)),
                pl.BlockSpec(memory_space=pl.ANY),
            ],
            out_specs=pl.BlockSpec((n_blocks, bl, lanes), lambda i, p: (0, 0, 0)),
            scratch_shapes=[pltpu.VMEM((n_blocks * n_slots, bl, lanes), table.dtype), pltpu.SemaphoreType.DMA((n_blocks * n_slots,))],
        ),
        interpret=interpret,
    )(pattern, weights, factors, seed, table)


def gather_columns(x):
    rows_here, width = x.shape
    same_core = lax.all_gather(x, "chip", tiled=True).reshape(-1, BLOCK, width)
    other_core = lax.ppermute(same_core, "core", [(0, 1), (1, 0)])
    return same_core, other_core


def body(embeds, labels, sharpness, pattern, mask_pos):
    rows_here, width = embeds.shape
    classes = labels.shape[1]
    n_col = lax.axis_size(COL)
    n_row = lax.axis_size("row")
    row_pos = lax.axis_index("row")
    blocks_here = rows_here // BLOCK
    slots_here = SLOTS // n_row
    span = slots_here * BLOCK
    per_device = classes // n_row
    owners = pattern // blocks_here
    local_ids = pattern % blocks_here
    my_owners = lax.dynamic_slice_in_dim(owners, row_pos * slots_here, slots_here, 1)
    my_ids = lax.dynamic_slice_in_dim(local_ids, row_pos * slots_here, slots_here, 1)
    peers = jnp.arange(n_col, dtype=jnp.int32)
    wanted = jnp.max(jnp.where(my_owners[..., None] == peers, my_ids[..., None], 0), axis=(0, 1))
    requested = lax.all_to_all(wanted, COL, split_axis=0, concat_axis=0, tiled=True)
    embedding_tiles = embeds.reshape(blocks_here, BLOCK, width)
    send_emb = embedding_tiles[requested]
    my_labels = lax.dynamic_slice_in_dim(labels, row_pos * per_device, per_device, 1)
    lanes = -(-per_device // 128) * 128
    my_labels = jnp.pad(my_labels, ((0, 0), (0, lanes - per_device)))
    all_labels = gather_columns(my_labels)
    shifted = mask_pos - row_pos * span
    shifted = jnp.where((shifted >= 0) & (shifted < span), shifted, span)
    positions = jnp.arange(span, dtype=jnp.int32)
    in_mask = jnp.any(shifted[:, :, None] == positions[None, None, :], axis=1)
    in_mask = in_mask.reshape(blocks_here, BLOCK, span)

    fetched_emb = lax.all_to_all(send_emb, COL, split_axis=0, concat_axis=0, tiled=True)
    candidate_ids = fetched_emb[my_owners].reshape(blocks_here, span, width)
    scores = jnp.einsum(
        "evg,erg->evr", embedding_tiles, candidate_ids, preferred_element_type=jnp.float32
    ) / math.sqrt(width)
    logits = scores * sharpness.reshape(blocks_here, BLOCK, 1)
    local_max = jnp.max(jnp.where(in_mask, logits, lowest_logit), axis=2)
    local_sum = jnp.sum(jnp.where(in_mask, jnp.exp(logits - local_max[..., None]), 0.0), axis=2)
    local_weights = jnp.where(
        in_mask, jnp.exp(logits - local_max[..., None]), 0.0
    ).astype(jnp.bfloat16)
    stats = lax.all_gather(jnp.stack([local_max, local_sum]), "row")
    all_weights = lax.all_gather(local_weights, "row")
    top = jnp.max(stats[:, 0], axis=0)
    totals = jnp.sum(stats[:, 1] * jnp.exp(stats[:, 0] - top), axis=0)
    factors = jnp.exp(stats[:, 0] - top) / totals

    shard_of = pattern // blocks_here
    on_this_core = (shard_of % 2 == lax.axis_index("core"))[..., None, None]
    pair_ids = (shard_of // 2) * blocks_here + pattern % blocks_here

    def propagate_using(gathered, seed):
        same_core, other_core = gathered
        candidates = jnp.where(on_this_core, same_core[pair_ids], other_core[pair_ids])
        candidates = candidates.reshape(blocks_here, n_row, span, lanes)
        pieces = jnp.einsum(
            "gtmk,tgkc->gtmc", all_weights, candidates, preferred_element_type=jnp.float32
        )
        pieces = (pieces * factors[..., None]).astype(jnp.bfloat16)
        summed = jnp.sum(pieces.astype(jnp.float32), axis=0).reshape(rows_here, lanes)
        return (mixing * summed + (1.0 - mixing) * seed.astype(jnp.float32)).astype(jnp.bfloat16)

    spread = propagate_using(all_labels, my_labels)
    whole_spread = lax.all_gather(spread, COL, tiled=True).reshape(-1, BLOCK, lanes)
    blended = fused_round(
        pattern, all_weights, factors[..., None], my_labels.reshape(blocks_here, BLOCK, lanes),
        whole_spread, mixing=mixing,
    )
    return blended.reshape(rows_here, lanes)[:, :per_device]


def solution(mesh):
    devices = mesh.devices
    fine = jax.sharding.Mesh(
        devices.reshape(devices.shape[0], devices.shape[1] // 2, 2), ("row", "chip", "core")
    )
    placed = (P(COL, None), P(COL, None), P(COL), P(COL, None), P(COL, None))
    return jax.shard_map(
        body, mesh=fine, in_specs=placed, out_specs=P(COL, "row"), check_vma=False
    )
```

```python
import functools
import math

import jax
import jax.numpy as jnp
from jax import lax
from jax.experimental import pallas as pl
from jax.experimental.pallas import tpu as pltpu
from jax.sharding import PartitionSpec as P

BLOCK = 128
SLOTS = 16


mixing = 0.75
lowest_logit = -1e30


COL = ("chip", "core")


def round_kernel(pat_ref, w_ref, f_ref, seed_ref, table_hbm, out_ref, buf, sems, *, n_blocks, n_groups, per_group, mixing):
    n_slots = n_groups * per_group
    copies = []
    for t in range(n_blocks):
        for slot in range(n_slots):
            idx = t * n_slots + slot
            c = pltpu.make_async_copy(table_hbm.at[pat_ref[t, slot]], buf.at[idx], sems.at[idx])
            c.start()
            copies.append(c)
    bl = buf.shape[1]
    for t in range(n_blocks):
        total = jnp.zeros(out_ref.shape[1:], jnp.float32)
        for g in range(n_groups):
            first = t * n_slots + g * per_group
            for s in range(per_group):
                copies[first + s].wait()
            candidates = buf[first:first + per_group].reshape(per_group * bl, buf.shape[2])
            acc = jnp.dot(w_ref[g, t], candidates, preferred_element_type=jnp.float32)
            total = total + (acc * f_ref[g, t]).astype(jnp.bfloat16).astype(jnp.float32)
        out_ref[t] = (mixing * total + (1.0 - mixing) * seed_ref[t].astype(jnp.float32)).astype(out_ref.dtype)

def fused_round(pattern, weights, factors, seed, table, mixing=0.75, interpret=False):
    n_groups, n_blocks, bl, span = weights.shape
    per_group = span // bl
    lanes = table.shape[-1]
    n_slots = n_groups * per_group
    kern = functools.partial(round_kernel, n_blocks=n_blocks, n_groups=n_groups, per_group=per_group, mixing=mixing)
    return pl.pallas_call(
        kern,
        out_shape=jax.ShapeDtypeStruct((n_blocks, bl, lanes), seed.dtype),
        grid_spec=pltpu.PrefetchScalarGridSpec(
            num_scalar_prefetch=1,
            grid=(1,),
            in_specs=[
                pl.BlockSpec(weights.shape, lambda i, p: (0, 0, 0, 0)),
                pl.BlockSpec(factors.shape, lambda i, p: (0, 0, 0, 0)),
                pl.BlockSpec(seed.shape, lambda i, p: (0, 0, 0)),
                pl.BlockSpec(memory_space=pl.ANY),
            ],
            out_specs=pl.BlockSpec((n_blocks, bl, lanes), lambda i, p: (0, 0, 0)),
            scratch_shapes=[pltpu.VMEM((n_blocks * n_slots, bl, lanes), table.dtype), pltpu.SemaphoreType.DMA((n_blocks * n_slots,))],
        ),
        interpret=interpret,
    )(pattern, weights, factors, seed, table)


def gather_columns(x):
    rows_here, width = x.shape
    same_core = lax.all_gather(x, "chip", tiled=True).reshape(-1, BLOCK, width)
    other_core = lax.ppermute(same_core, "core", [(0, 1), (1, 0)])
    return same_core, other_core


def body(embeds, labels, sharpness, pattern, mask_pos):
    rows_here, width = embeds.shape
    classes = labels.shape[1]
    n_col = lax.axis_size(COL)
    n_row = lax.axis_size("row")
    row_pos = lax.axis_index("row")
    blocks_here = rows_here // BLOCK
    slots_here = SLOTS // n_row
    span = slots_here * BLOCK
    per_device = classes // n_row
    owners = pattern // blocks_here
    local_ids = pattern % blocks_here
    my_owners = lax.dynamic_slice_in_dim(owners, row_pos * slots_here, slots_here, 1)
    my_ids = lax.dynamic_slice_in_dim(local_ids, row_pos * slots_here, slots_here, 1)
    peers = jnp.arange(n_col, dtype=jnp.int32)
    wanted = jnp.max(jnp.where(my_owners[..., None] == peers, my_ids[..., None], 0), axis=(0, 1))
    requested = lax.all_to_all(wanted, COL, split_axis=0, concat_axis=0, tiled=True)
    embedding_tiles = embeds.reshape(blocks_here, BLOCK, width)
    send_emb = embedding_tiles[requested]
    my_labels = lax.dynamic_slice_in_dim(labels, row_pos * per_device, per_device, 1)
    lanes = -(-per_device // 128) * 128
    my_labels = jnp.pad(my_labels, ((0, 0), (0, lanes - per_device)))
    all_labels = gather_columns(my_labels)
    shifted = mask_pos - row_pos * span
    shifted = jnp.where((shifted >= 0) & (shifted < span), shifted, span)
    positions = jnp.arange(span, dtype=jnp.int32)
    in_mask = jnp.any(shifted[:, :, None] == positions[None, None, :], axis=1)
    in_mask = in_mask.reshape(blocks_here, BLOCK, span)

    fetched_emb = lax.all_to_all(send_emb, COL, split_axis=0, concat_axis=0, tiled=True)
    candidate_ids = fetched_emb[my_owners].reshape(blocks_here, span, width)
    scores = jnp.einsum(
        "evg,erg->evr", embedding_tiles, candidate_ids, preferred_element_type=jnp.float32
    ) / math.sqrt(width)
    logits = scores * sharpness.reshape(blocks_here, BLOCK, 1)
    local_max = jnp.max(jnp.where(in_mask, logits, lowest_logit), axis=2)
    local_sum = jnp.sum(jnp.where(in_mask, jnp.exp(logits - local_max[..., None]), 0.0), axis=2)
    local_weights = jnp.where(
        in_mask, jnp.exp(logits - local_max[..., None]), 0.0
    ).astype(jnp.bfloat16)
    stats = lax.all_gather(jnp.stack([local_max, local_sum]), "row")
    all_weights = lax.all_gather(local_weights, "row")
    top = jnp.max(stats[:, 0], axis=0)
    totals = jnp.sum(stats[:, 1] * jnp.exp(stats[:, 0] - top), axis=0)
    factors = jnp.exp(stats[:, 0] - top) / totals

    shard_of = pattern // blocks_here
    on_this_core = (shard_of % 2 == lax.axis_index("core"))[..., None, None]
    pair_ids = (shard_of // 2) * blocks_here + pattern % blocks_here

    def propagate_using(gathered, seed):
        same_core, other_core = gathered
        candidates = jnp.where(on_this_core, same_core[pair_ids], other_core[pair_ids])
        candidates = candidates.reshape(blocks_here, n_row, span, lanes)
        pieces = jnp.einsum(
            "gtmk,tgkc->gtmc", all_weights, candidates, preferred_element_type=jnp.float32
        )
        pieces = (pieces * factors[..., None]).astype(jnp.bfloat16)
        summed = jnp.sum(pieces.astype(jnp.float32), axis=0).reshape(rows_here, lanes)
        return (mixing * summed + (1.0 - mixing) * seed.astype(jnp.float32)).astype(jnp.bfloat16)

    spread = propagate_using(all_labels, my_labels)
    whole_spread = lax.all_gather(spread, COL, tiled=True).reshape(-1, BLOCK, lanes)
    blended = fused_round(
        pattern, all_weights, factors[..., None], my_labels.reshape(blocks_here, BLOCK, lanes),
        whole_spread, mixing=mixing,
    )
    return blended.reshape(rows_here, lanes)[:, :per_device]


def solution(mesh):
    devices = mesh.devices
    fine = jax.sharding.Mesh(
        devices.reshape(devices.shape[0], devices.shape[1] // 2, 2), ("row", "chip", "core")
    )
    placed = (P(COL, None), P(COL, None), P(COL), P(COL, None), P(COL, None))
    return jax.shard_map(
        body, mesh=fine, in_specs=placed, out_specs=P(COL, "row"), check_vma=False
    )
```

```python
import math

import jax
import jax.numpy as jnp
from jax import lax
from jax.sharding import PartitionSpec as P

BLOCK = 128
SLOTS = 16


mixing = 0.75
lowest_logit = -1e30


COL = ("chip", "core")


def gather_columns(x):
    rows_here, width = x.shape
    same_core = lax.all_gather(x, "chip", tiled=True).reshape(-1, BLOCK, width)
    other_core = lax.ppermute(same_core, "core", [(0, 1), (1, 0)])
    return same_core, other_core


def body(embeds, labels, sharpness, pattern, mask_pos):
    rows_here, width = embeds.shape
    classes = labels.shape[1]
    n_col = lax.axis_size(COL)
    n_row = lax.axis_size("row")
    row_pos = lax.axis_index("row")
    blocks_here = rows_here // BLOCK
    slots_here = SLOTS // n_row
    span = slots_here * BLOCK
    per_device = classes // n_row
    owners = pattern // blocks_here
    local_ids = pattern % blocks_here
    my_owners = lax.dynamic_slice_in_dim(owners, row_pos * slots_here, slots_here, 1)
    my_ids = lax.dynamic_slice_in_dim(local_ids, row_pos * slots_here, slots_here, 1)
    peers = jnp.arange(n_col, dtype=jnp.int32)
    wanted = jnp.max(jnp.where(my_owners[..., None] == peers, my_ids[..., None], 0), axis=(0, 1))
    requested = lax.all_to_all(wanted, COL, split_axis=0, concat_axis=0, tiled=True)
    embedding_tiles = embeds.reshape(blocks_here, BLOCK, width)
    send_emb = embedding_tiles[requested]
    my_labels = lax.dynamic_slice_in_dim(labels, row_pos * per_device, per_device, 1)
    lanes = -(-per_device // 128) * 128
    my_labels = jnp.pad(my_labels, ((0, 0), (0, lanes - per_device)))
    all_labels = gather_columns(my_labels)
    shifted = mask_pos - row_pos * span
    shifted = jnp.where((shifted >= 0) & (shifted < span), shifted, span)
    positions = jnp.arange(span, dtype=jnp.int32)
    in_mask = jnp.any(shifted[:, :, None] == positions[None, None, :], axis=1)
    in_mask = in_mask.reshape(blocks_here, BLOCK, span)

    fetched_emb = lax.all_to_all(send_emb, COL, split_axis=0, concat_axis=0, tiled=True)
    candidate_ids = fetched_emb[my_owners].reshape(blocks_here, span, width)
    scores = jnp.einsum(
        "evg,erg->evr", embedding_tiles, candidate_ids, preferred_element_type=jnp.float32
    ) / math.sqrt(width)
    logits = scores * sharpness.reshape(blocks_here, BLOCK, 1)
    local_max = jnp.max(jnp.where(in_mask, logits, lowest_logit), axis=2)
    local_sum = jnp.sum(jnp.where(in_mask, jnp.exp(logits - local_max[..., None]), 0.0), axis=2)
    local_weights = jnp.where(
        in_mask, jnp.exp(logits - local_max[..., None]), 0.0
    ).astype(jnp.bfloat16)
    stats = lax.all_gather(jnp.stack([local_max, local_sum]), "row")
    all_weights = lax.all_gather(local_weights, "row")
    top = jnp.max(stats[:, 0], axis=0)
    totals = jnp.sum(stats[:, 1] * jnp.exp(stats[:, 0] - top), axis=0)
    factors = jnp.exp(stats[:, 0] - top) / totals

    shard_of = pattern // blocks_here
    on_this_core = (shard_of % 2 == lax.axis_index("core"))[..., None, None]
    pair_ids = (shard_of // 2) * blocks_here + pattern % blocks_here

    def propagate_using(gathered, seed, whole=False):
        if whole:
            blocks_all = gathered.shape[0]
            picks = (pattern.reshape(-1, 1) == jnp.arange(blocks_all, dtype=jnp.int32)).astype(gathered.dtype)
            candidates = jnp.dot(
                picks, gathered.reshape(blocks_all, -1), preferred_element_type=jnp.float32
            ).astype(gathered.dtype).reshape(pattern.shape + gathered.shape[1:])
        else:
            same_core, other_core = gathered
            candidates = jnp.where(on_this_core, same_core[pair_ids], other_core[pair_ids])
        candidates = candidates.reshape(blocks_here, n_row, span, lanes)
        pieces = jnp.einsum(
            "gtmk,tgkc->gtmc", all_weights, candidates, preferred_element_type=jnp.float32
        )
        pieces = (pieces * factors[..., None]).astype(jnp.bfloat16)
        summed = jnp.sum(pieces.astype(jnp.float32), axis=0).reshape(rows_here, lanes)
        return (mixing * summed + (1.0 - mixing) * seed.astype(jnp.float32)).astype(jnp.bfloat16)

    spread = propagate_using(all_labels, my_labels)
    whole_spread = lax.all_gather(spread, COL, tiled=True).reshape(-1, BLOCK, lanes)
    return propagate_using(whole_spread, my_labels, whole=True)[:, :per_device]


def solution(mesh):
    devices = mesh.devices
    fine = jax.sharding.Mesh(
        devices.reshape(devices.shape[0], devices.shape[1] // 2, 2), ("row", "chip", "core")
    )
    placed = (P(COL, None), P(COL, None), P(COL), P(COL, None), P(COL, None))
    return jax.shard_map(
        body, mesh=fine, in_specs=placed, out_specs=P(COL, "row"), check_vma=False
    )
```

```python
import math

import jax
import jax.numpy as jnp
from jax import lax
from jax.sharding import PartitionSpec as P

BLOCK = 128
SLOTS = 16


mixing = 0.75
lowest_logit = -1e30


COL = ("chip", "core")


def gather_columns(x):
    rows_here, width = x.shape
    same_core = lax.all_gather(x, "chip", tiled=True).reshape(-1, BLOCK, width)
    other_core = lax.ppermute(same_core, "core", [(0, 1), (1, 0)])
    return same_core, other_core


def body(embeds, labels, sharpness, pattern, mask_pos):
    rows_here, width = embeds.shape
    classes = labels.shape[1]
    n_col = lax.axis_size(COL)
    n_row = lax.axis_size("row")
    row_pos = lax.axis_index("row")
    blocks_here = rows_here // BLOCK
    slots_here = SLOTS // n_row
    span = slots_here * BLOCK
    per_device = classes // n_row
    owners = pattern // blocks_here
    local_ids = pattern % blocks_here
    my_owners = lax.dynamic_slice_in_dim(owners, row_pos * slots_here, slots_here, 1)
    my_ids = lax.dynamic_slice_in_dim(local_ids, row_pos * slots_here, slots_here, 1)
    peers = jnp.arange(n_col, dtype=jnp.int32)
    wanted = jnp.max(jnp.where(my_owners[..., None] == peers, my_ids[..., None], 0), axis=(0, 1))
    requested = lax.all_to_all(wanted, COL, split_axis=0, concat_axis=0, tiled=True)
    embedding_tiles = embeds.reshape(blocks_here, BLOCK, width)
    send_emb = embedding_tiles[requested]
    my_labels = lax.dynamic_slice_in_dim(labels, row_pos * per_device, per_device, 1)
    lanes = -(-per_device // 128) * 128
    my_labels = jnp.pad(my_labels, ((0, 0), (0, lanes - per_device)))
    all_labels = gather_columns(my_labels)
    shifted = mask_pos - row_pos * span
    shifted = jnp.where((shifted >= 0) & (shifted < span), shifted, span)
    positions = jnp.arange(span, dtype=jnp.int32)
    in_mask = jnp.any(shifted[:, :, None] == positions[None, None, :], axis=1)
    in_mask = in_mask.reshape(blocks_here, BLOCK, span)

    fetched_emb = lax.all_to_all(send_emb, COL, split_axis=0, concat_axis=0, tiled=True)
    candidate_ids = fetched_emb[my_owners].reshape(blocks_here, span, width)
    scores = jnp.einsum(
        "evg,erg->evr", embedding_tiles, candidate_ids, preferred_element_type=jnp.float32
    ) / math.sqrt(width)
    logits = scores * sharpness.reshape(blocks_here, BLOCK, 1)
    local_max = jnp.max(jnp.where(in_mask, logits, lowest_logit), axis=2)
    local_sum = jnp.sum(jnp.where(in_mask, jnp.exp(logits - local_max[..., None]), 0.0), axis=2)
    local_weights = jnp.where(
        in_mask, jnp.exp(logits - local_max[..., None]), 0.0
    ).astype(jnp.bfloat16)
    stats = lax.all_gather(jnp.stack([local_max, local_sum]), "row")
    all_weights = lax.all_gather(local_weights, "row")
    top = jnp.max(stats[:, 0], axis=0)
    totals = jnp.sum(stats[:, 1] * jnp.exp(stats[:, 0] - top), axis=0)
    factors = jnp.exp(stats[:, 0] - top) / totals

    shard_of = pattern // blocks_here
    on_this_core = (shard_of % 2 == lax.axis_index("core"))[..., None, None]
    pair_ids = (shard_of // 2) * blocks_here + pattern % blocks_here

    row_weights = (all_weights * factors[..., None]).astype(jnp.bfloat16)

    def propagate_using(gathered, seed, whole=False):
        if whole:
            candidates = gathered[pattern]
        else:
            same_core, other_core = gathered
            candidates = jnp.where(on_this_core, same_core[pair_ids], other_core[pair_ids])
        candidates = candidates.reshape(blocks_here, n_row, span, lanes)
        summed = jnp.einsum(
            "gtmk,tgkc->tmc", row_weights, candidates, preferred_element_type=jnp.float32
        ).reshape(rows_here, lanes)
        return (mixing * summed + (1.0 - mixing) * seed.astype(jnp.float32)).astype(jnp.bfloat16)

    spread = propagate_using(all_labels, my_labels)
    whole_spread = lax.all_gather(spread, COL, tiled=True).reshape(-1, BLOCK, lanes)
    return propagate_using(whole_spread, my_labels, whole=True)[:, :per_device]


def solution(mesh):
    devices = mesh.devices
    fine = jax.sharding.Mesh(
        devices.reshape(devices.shape[0], devices.shape[1] // 2, 2), ("row", "chip", "core")
    )
    placed = (P(COL, None), P(COL, None), P(COL), P(COL, None), P(COL, None))
    return jax.shard_map(
        body, mesh=fine, in_specs=placed, out_specs=P(COL, "row"), check_vma=False
    )
```

```python
import math

import jax
import jax.numpy as jnp
from jax import lax
from jax.sharding import PartitionSpec as P

BLOCK = 128
SLOTS = 16


mixing = 0.75
lowest_logit = -1e30


COL = ("chip", "core")


def gather_columns(x):
    rows_here, width = x.shape
    same_core = lax.all_gather(x, "chip", tiled=True).reshape(-1, BLOCK, width)
    other_core = lax.ppermute(same_core, "core", [(0, 1), (1, 0)])
    return same_core, other_core


def body(embeds, labels, sharpness, pattern, mask_pos):
    rows_here, width = embeds.shape
    classes = labels.shape[1]
    n_col = lax.axis_size(COL)
    n_row = lax.axis_size("row")
    row_pos = lax.axis_index("row")
    blocks_here = rows_here // BLOCK
    slots_here = SLOTS // n_row
    span = slots_here * BLOCK
    per_device = classes // n_row
    owners = pattern // blocks_here
    local_ids = pattern % blocks_here
    my_owners = lax.dynamic_slice_in_dim(owners, row_pos * slots_here, slots_here, 1)
    my_ids = lax.dynamic_slice_in_dim(local_ids, row_pos * slots_here, slots_here, 1)
    peers = jnp.arange(n_col, dtype=jnp.int32)
    wanted = jnp.max(jnp.where(my_owners[..., None] == peers, my_ids[..., None], 0), axis=(0, 1))
    requested = lax.all_to_all(wanted, COL, split_axis=0, concat_axis=0, tiled=True)
    embedding_tiles = embeds.reshape(blocks_here, BLOCK, width)
    send_emb = embedding_tiles[requested]
    my_labels = lax.dynamic_slice_in_dim(labels, row_pos * per_device, per_device, 1)
    lanes = -(-per_device // 128) * 128
    my_labels = jnp.pad(my_labels, ((0, 0), (0, lanes - per_device)))
    all_labels = gather_columns(my_labels)
    shifted = mask_pos - row_pos * span
    shifted = jnp.where((shifted >= 0) & (shifted < span), shifted, span)
    positions = jnp.arange(span, dtype=jnp.int32)
    in_mask = jnp.any(shifted[:, :, None] == positions[None, None, :], axis=1)
    in_mask = in_mask.reshape(blocks_here, BLOCK, span)

    half = width // 2
    scores = 0.0
    for lo, hi in ((0, half), (half, width)):
        fetched_emb = lax.all_to_all(send_emb[..., lo:hi], COL, split_axis=0, concat_axis=0, tiled=True)
        candidate_ids = fetched_emb[my_owners].reshape(blocks_here, span, hi - lo)
        scores = scores + jnp.einsum(
            "evg,erg->evr", embedding_tiles[..., lo:hi], candidate_ids,
            preferred_element_type=jnp.float32,
        )
    scores = scores / math.sqrt(width)
    logits = scores * sharpness.reshape(blocks_here, BLOCK, 1)
    local_max = jnp.max(jnp.where(in_mask, logits, lowest_logit), axis=2)
    local_sum = jnp.sum(jnp.where(in_mask, jnp.exp(logits - local_max[..., None]), 0.0), axis=2)
    local_weights = jnp.where(
        in_mask, jnp.exp(logits - local_max[..., None]), 0.0
    ).astype(jnp.bfloat16)
    stats = lax.all_gather(jnp.stack([local_max, local_sum]), "row")
    all_weights = lax.all_gather(local_weights, "row")
    top = jnp.max(stats[:, 0], axis=0)
    totals = jnp.sum(stats[:, 1] * jnp.exp(stats[:, 0] - top), axis=0)
    factors = jnp.exp(stats[:, 0] - top) / totals

    shard_of = pattern // blocks_here
    on_this_core = (shard_of % 2 == lax.axis_index("core"))[..., None, None]
    pair_ids = (shard_of // 2) * blocks_here + pattern % blocks_here

    def propagate_using(gathered, seed, whole=False):
        if whole:
            candidates = gathered[pattern]
        else:
            same_core, other_core = gathered
            candidates = jnp.where(on_this_core, same_core[pair_ids], other_core[pair_ids])
        candidates = candidates.reshape(blocks_here, n_row, span, lanes)
        pieces = jnp.einsum(
            "gtmk,tgkc->gtmc", all_weights, candidates, preferred_element_type=jnp.float32
        )
        pieces = (pieces * factors[..., None]).astype(jnp.bfloat16)
        summed = jnp.sum(pieces.astype(jnp.float32), axis=0).reshape(rows_here, lanes)
        return (mixing * summed + (1.0 - mixing) * seed.astype(jnp.float32)).astype(jnp.bfloat16)

    spread = propagate_using(all_labels, my_labels)
    whole_spread = lax.all_gather(spread, COL, tiled=True).reshape(-1, BLOCK, lanes)
    return propagate_using(whole_spread, my_labels, whole=True)[:, :per_device]


def solution(mesh):
    devices = mesh.devices
    fine = jax.sharding.Mesh(
        devices.reshape(devices.shape[0], devices.shape[1] // 2, 2), ("row", "chip", "core")
    )
    placed = (P(COL, None), P(COL, None), P(COL), P(COL, None), P(COL, None))
    return jax.shard_map(
        body, mesh=fine, in_specs=placed, out_specs=P(COL, "row"), check_vma=False
    )
```

```python
import math

import jax
import jax.numpy as jnp
from jax import lax
from jax.sharding import PartitionSpec as P

BLOCK = 128
SLOTS = 16


mixing = 0.75
lowest_logit = -1e30


COL = ("chip", "core")


def gather_columns(x):
    rows_here, width = x.shape
    same_core = lax.all_gather(x, "chip", tiled=True).reshape(-1, BLOCK, width)
    other_core = lax.ppermute(same_core, "core", [(0, 1), (1, 0)])
    return same_core, other_core


def body(embeds, labels, sharpness, pattern, mask_pos):
    rows_here, width = embeds.shape
    classes = labels.shape[1]
    n_col = lax.axis_size(COL)
    n_row = lax.axis_size("row")
    row_pos = lax.axis_index("row")
    blocks_here = rows_here // BLOCK
    slots_here = SLOTS // n_row
    span = slots_here * BLOCK
    per_device = classes // n_row
    owners = pattern // blocks_here
    local_ids = pattern % blocks_here
    my_owners = lax.dynamic_slice_in_dim(owners, row_pos * slots_here, slots_here, 1)
    my_ids = lax.dynamic_slice_in_dim(local_ids, row_pos * slots_here, slots_here, 1)
    peers = jnp.arange(n_col, dtype=jnp.int32)
    wanted = jnp.max(jnp.where(my_owners[..., None] == peers, my_ids[..., None], 0), axis=(0, 1))
    requested = lax.all_to_all(wanted, COL, split_axis=0, concat_axis=0, tiled=True)
    embedding_tiles = embeds.reshape(blocks_here, BLOCK, width)
    send_emb = embedding_tiles[requested]
    my_labels = lax.dynamic_slice_in_dim(labels, row_pos * per_device, per_device, 1)
    lanes = -(-per_device // 128) * 128
    my_labels = jnp.pad(my_labels, ((0, 0), (0, lanes - per_device)))
    all_labels = gather_columns(my_labels)
    shifted = mask_pos - row_pos * span
    shifted = jnp.where((shifted >= 0) & (shifted < span), shifted, span)
    positions = jnp.arange(span, dtype=jnp.int32)
    in_mask = jnp.any(shifted[:, :, None] == positions[None, None, :], axis=1)
    in_mask = in_mask.reshape(blocks_here, BLOCK, span)

    fetched_emb = lax.all_to_all(send_emb, COL, split_axis=0, concat_axis=0, tiled=True)
    candidate_ids = fetched_emb[my_owners].reshape(blocks_here, span, width)
    scores = jnp.einsum(
        "evg,erg->evr", embedding_tiles, candidate_ids, preferred_element_type=jnp.float32
    ) / math.sqrt(width)
    logits = scores * sharpness.reshape(blocks_here, BLOCK, 1)
    local_max = jnp.max(jnp.where(in_mask, logits, lowest_logit), axis=2)
    local_sum = jnp.sum(jnp.where(in_mask, jnp.exp(logits - local_max[..., None]), 0.0), axis=2)
    local_weights = jnp.where(
        in_mask, jnp.exp(logits - local_max[..., None]), 0.0
    ).astype(jnp.bfloat16)
    stats = lax.all_gather(jnp.stack([local_max, local_sum]), "row")
    all_weights = lax.all_gather(local_weights, "row")
    top = jnp.max(stats[:, 0], axis=0)
    totals = jnp.sum(stats[:, 1] * jnp.exp(stats[:, 0] - top), axis=0)
    factors = jnp.exp(stats[:, 0] - top) / totals

    shard_of = pattern // blocks_here
    on_this_core = (shard_of % 2 == lax.axis_index("core"))[..., None, None]
    pair_ids = (shard_of // 2) * blocks_here + pattern % blocks_here

    def propagate_using(gathered, seed, whole=False):
        gathered_lanes = seed.shape[-1]
        if whole:
            candidates = gathered[pattern]
        else:
            same_core, other_core = gathered
            candidates = jnp.where(on_this_core, same_core[pair_ids], other_core[pair_ids])
        candidates = candidates.reshape(blocks_here, n_row, span, gathered_lanes)
        pieces = jnp.einsum(
            "gtmk,tgkc->gtmc", all_weights, candidates, preferred_element_type=jnp.float32
        )
        pieces = (pieces * factors[..., None]).astype(jnp.bfloat16)
        summed = jnp.sum(pieces.astype(jnp.float32), axis=0).reshape(rows_here, gathered_lanes)
        return (mixing * summed + (1.0 - mixing) * seed.astype(jnp.float32)).astype(jnp.bfloat16)

    spread = propagate_using(all_labels, my_labels)
    whole_spread = lax.all_gather(spread[:, :per_device], COL, tiled=True)
    whole_spread = whole_spread.reshape(-1, BLOCK, per_device)
    return propagate_using(whole_spread, my_labels[:, :per_device], whole=True)


def solution(mesh):
    devices = mesh.devices
    fine = jax.sharding.Mesh(
        devices.reshape(devices.shape[0], devices.shape[1] // 2, 2), ("row", "chip", "core")
    )
    placed = (P(COL, None), P(COL, None), P(COL), P(COL, None), P(COL, None))
    return jax.shard_map(
        body, mesh=fine, in_specs=placed, out_specs=P(COL, "row"), check_vma=False
    )
```

```python
import math

import jax
import jax.numpy as jnp
from jax import lax
from jax.sharding import PartitionSpec as P

BLOCK = 128
SLOTS = 16


mixing = 0.75
lowest_logit = -1e30


COL = ("chip", "core")


def gather_columns(x):
    rows_here, width = x.shape
    same_core = lax.all_gather(x, "chip", tiled=True).reshape(-1, BLOCK, width)
    other_core = lax.ppermute(same_core, "core", [(0, 1), (1, 0)])
    return same_core, other_core


def body(embeds, labels, sharpness, pattern, mask_pos):
    rows_here, width = embeds.shape
    classes = labels.shape[1]
    n_col = lax.axis_size(COL)
    n_row = lax.axis_size("row")
    row_pos = lax.axis_index("row")
    blocks_here = rows_here // BLOCK
    slots_here = SLOTS // n_row
    span = slots_here * BLOCK
    per_device = classes // n_row
    owners = pattern // blocks_here
    local_ids = pattern % blocks_here
    my_owners = lax.dynamic_slice_in_dim(owners, row_pos * slots_here, slots_here, 1)
    my_ids = lax.dynamic_slice_in_dim(local_ids, row_pos * slots_here, slots_here, 1)
    peers = jnp.arange(n_col, dtype=jnp.int32)
    wanted = jnp.max(jnp.where(my_owners[..., None] == peers, my_ids[..., None], 0), axis=(0, 1))
    requested = lax.all_to_all(wanted, COL, split_axis=0, concat_axis=0, tiled=True)
    embedding_tiles = embeds.reshape(blocks_here, BLOCK, width)
    send_emb = embedding_tiles[requested]
    my_labels = lax.dynamic_slice_in_dim(labels, row_pos * per_device, per_device, 1)
    all_labels = gather_columns(my_labels)
    shifted = mask_pos - row_pos * span
    shifted = jnp.where((shifted >= 0) & (shifted < span), shifted, span)
    positions = jnp.arange(span, dtype=jnp.int32)
    in_mask = jnp.any(shifted[:, :, None] == positions[None, None, :], axis=1)
    in_mask = in_mask.reshape(blocks_here, BLOCK, span)

    fetched_emb = lax.all_to_all(send_emb, COL, split_axis=0, concat_axis=0, tiled=True)
    candidate_ids = fetched_emb[my_owners].reshape(blocks_here, span, width)
    scores = jnp.einsum(
        "evg,erg->evr", embedding_tiles, candidate_ids, preferred_element_type=jnp.float32
    ) / math.sqrt(width)
    logits = scores * sharpness.reshape(blocks_here, BLOCK, 1)
    local_max = jnp.max(jnp.where(in_mask, logits, lowest_logit), axis=2)
    local_sum = jnp.sum(jnp.where(in_mask, jnp.exp(logits - local_max[..., None]), 0.0), axis=2)
    local_weights = jnp.where(
        in_mask, jnp.exp(logits - local_max[..., None]), 0.0
    ).astype(jnp.bfloat16)
    stats = lax.all_gather(jnp.stack([local_max, local_sum]), "row")
    all_weights = lax.all_gather(local_weights, "row")
    top = jnp.max(stats[:, 0], axis=0)
    totals = jnp.sum(stats[:, 1] * jnp.exp(stats[:, 0] - top), axis=0)
    factors = jnp.exp(stats[:, 0] - top) / totals

    shard_of = pattern // blocks_here
    on_this_core = (shard_of % 2 == lax.axis_index("core"))[..., None, None]
    pair_ids = (shard_of // 2) * blocks_here + pattern % blocks_here

    def propagate_using(gathered, seed, whole=False):
        gathered_lanes = seed.shape[-1]
        if whole:
            candidates = gathered[pattern]
        else:
            same_core, other_core = gathered
            candidates = jnp.where(on_this_core, same_core[pair_ids], other_core[pair_ids])
        candidates = candidates.reshape(blocks_here, n_row, span, gathered_lanes)
        pieces = jnp.einsum(
            "gtmk,tgkc->gtmc", all_weights, candidates, preferred_element_type=jnp.float32
        )
        pieces = (pieces * factors[..., None]).astype(jnp.bfloat16)
        summed = jnp.sum(pieces.astype(jnp.float32), axis=0).reshape(rows_here, gathered_lanes)
        return (mixing * summed + (1.0 - mixing) * seed.astype(jnp.float32)).astype(jnp.bfloat16)

    spread = propagate_using(all_labels, my_labels)
    whole_spread = lax.all_gather(spread[:, :per_device], COL, tiled=True)
    whole_spread = whole_spread.reshape(-1, BLOCK, per_device)
    return propagate_using(whole_spread, my_labels[:, :per_device], whole=True)


def solution(mesh):
    devices = mesh.devices
    fine = jax.sharding.Mesh(
        devices.reshape(devices.shape[0], devices.shape[1] // 2, 2), ("row", "chip", "core")
    )
    placed = (P(COL, None), P(COL, None), P(COL), P(COL, None), P(COL, None))
    return jax.shard_map(
        body, mesh=fine, in_specs=placed, out_specs=P(COL, "row"), check_vma=False
    )
```

```python
import math

import jax
import jax.numpy as jnp
from jax import lax
from jax.sharding import PartitionSpec as P

BLOCK = 128
SLOTS = 16


mixing = 0.75
lowest_logit = -1e30


COL = ("chip", "core")


def gather_columns(x):
    rows_here, width = x.shape
    same_core = lax.all_gather(x, "chip", tiled=True).reshape(-1, BLOCK, width)
    other_core = lax.ppermute(same_core, "core", [(0, 1), (1, 0)])
    return same_core, other_core


def body(embeds, labels, sharpness, pattern, mask_pos):
    rows_here, width = embeds.shape
    classes = labels.shape[1]
    n_col = lax.axis_size(COL)
    n_row = lax.axis_size("row")
    row_pos = lax.axis_index("row")
    blocks_here = rows_here // BLOCK
    slots_here = SLOTS // n_row
    span = slots_here * BLOCK
    per_device = classes // n_row
    owners = pattern // blocks_here
    local_ids = pattern % blocks_here
    my_owners = lax.dynamic_slice_in_dim(owners, row_pos * slots_here, slots_here, 1)
    my_ids = lax.dynamic_slice_in_dim(local_ids, row_pos * slots_here, slots_here, 1)
    peers = jnp.arange(n_col, dtype=jnp.int32)
    wanted = jnp.max(jnp.where(my_owners[..., None] == peers, my_ids[..., None], 0), axis=(0, 1))
    requested = lax.all_to_all(wanted, COL, split_axis=0, concat_axis=0, tiled=True)
    embedding_tiles = embeds.reshape(blocks_here, BLOCK, width)
    send_emb = embedding_tiles[requested]
    my_labels = lax.dynamic_slice_in_dim(labels, row_pos * per_device, per_device, 1)
    lanes = -(-per_device // 128) * 128
    my_labels = jnp.pad(my_labels, ((0, 0), (0, lanes - per_device)))
    all_labels = gather_columns(my_labels)
    shifted = mask_pos - row_pos * span
    shifted = jnp.where((shifted >= 0) & (shifted < span), shifted, span)
    positions = jnp.arange(span, dtype=jnp.int32)
    in_mask = jnp.any(shifted[:, :, None] == positions[None, None, :], axis=1)
    in_mask = in_mask.reshape(blocks_here, BLOCK, span)

    fetched_emb = lax.all_to_all(send_emb, COL, split_axis=0, concat_axis=0, tiled=True)
    candidate_ids = jnp.stack([
        lax.dynamic_index_in_dim(fetched_emb, my_owners[t, s], 0, keepdims=False)
        for t in range(blocks_here) for s in range(slots_here)
    ]).reshape(blocks_here, span, width)
    scores = jnp.einsum(
        "evg,erg->evr", embedding_tiles, candidate_ids, preferred_element_type=jnp.float32
    ) / math.sqrt(width)
    logits = scores * sharpness.reshape(blocks_here, BLOCK, 1)
    local_max = jnp.max(jnp.where(in_mask, logits, lowest_logit), axis=2)
    local_sum = jnp.sum(jnp.where(in_mask, jnp.exp(logits - local_max[..., None]), 0.0), axis=2)
    local_weights = jnp.where(
        in_mask, jnp.exp(logits - local_max[..., None]), 0.0
    ).astype(jnp.bfloat16)
    stats = lax.all_gather(jnp.stack([local_max, local_sum]), "row")
    all_weights = lax.all_gather(local_weights, "row")
    top = jnp.max(stats[:, 0], axis=0)
    totals = jnp.sum(stats[:, 1] * jnp.exp(stats[:, 0] - top), axis=0)
    factors = jnp.exp(stats[:, 0] - top) / totals

    shard_of = pattern // blocks_here
    on_this_core = (shard_of % 2 == lax.axis_index("core"))[..., None, None]
    pair_ids = (shard_of // 2) * blocks_here + pattern % blocks_here

    def propagate_using(gathered, seed, whole=False):
        gathered_lanes = seed.shape[-1]
        if whole:
            candidates = gathered[pattern]
        else:
            same_core, other_core = gathered
            candidates = jnp.where(on_this_core, same_core[pair_ids], other_core[pair_ids])
        candidates = candidates.reshape(blocks_here, n_row, span, gathered_lanes)
        pieces = jnp.einsum(
            "gtmk,tgkc->gtmc", all_weights, candidates, preferred_element_type=jnp.float32
        )
        pieces = (pieces * factors[..., None]).astype(jnp.bfloat16)
        summed = jnp.sum(pieces.astype(jnp.float32), axis=0).reshape(rows_here, gathered_lanes)
        return (mixing * summed + (1.0 - mixing) * seed.astype(jnp.float32)).astype(jnp.bfloat16)

    spread = propagate_using(all_labels, my_labels)
    whole_spread = lax.all_gather(spread[:, :per_device], COL, tiled=True)
    whole_spread = whole_spread.reshape(-1, BLOCK, per_device)
    return propagate_using(whole_spread, my_labels[:, :per_device], whole=True)


def solution(mesh):
    devices = mesh.devices
    fine = jax.sharding.Mesh(
        devices.reshape(devices.shape[0], devices.shape[1] // 2, 2), ("row", "chip", "core")
    )
    placed = (P(COL, None), P(COL, None), P(COL), P(COL, None), P(COL, None))
    return jax.shard_map(
        body, mesh=fine, in_specs=placed, out_specs=P(COL, "row"), check_vma=False
    )
```
